1024 devices in a mesh: dp: 32 (over z_lo, y), expert: 32 (over x, z_hi, core).
Axes of the slice: x: 4, y: 4, z: 32 (z_hi: 4, z_lo: 8; z = z_hi * 8 + z_lo), core: 2. Of those that a mesh axis runs over, the one named last changes fastest.
Arguments:
- tokens: bfloat16 [131072, 2048], P(('dp', 'expert')), may hold values from -6 to 6
- hot_gate: float32 [131072], P(('dp', 'expert')), may hold values from 0.3 to 1
- cold_expert: int32 [32768, 1], P(('dp', 'expert')), may hold values from 0 to 31; in each aligned block of 32 rows (0 to 31, 32 to 63, ...) at most 2 rows name the same one
- cold_gate: float32 [32768], P(('dp', 'expert')), may hold values from 0.3 to 1
- hot_id: int32 [1], replicated, may hold values from 0 to 131071
- w_gate: bfloat16 [32, 2048, 384], P('expert'), may hold values from -0.125 to 0.125
- w_up: bfloat16 [32, 2048, 384], P('expert'), may hold values from -0.125 to 0.125
- w_down: bfloat16 [32, 384, 2048], P('expert'), may hold values from -0.3125 to 0.3125
Outputs:
- mixed: bfloat16 [131072, 2048], P(('dp', 'expert'))
The draws below stay inside these ranges and needn't reach their ends.
Inputs may be any that keep to these rules, and one draw needn't show every extreme that they name: Among the 32 dispatched tokens of one device (aligned blocks of cold_expert), no expert is named more than 2 times, and in every draw some device names some expert exactly 2 times.
All inputs are finite; a program needn't handle non-finite values.
Results may differ from the reference program's by a relative error of at most 0.0053.
Values may be sent and summed in bfloat16 or wider, within the bound.
No kernel may reach another device: no remote copies, remote signals or barrier semaphores. Data moves between devices by JAX's collectives and lax.ppermute only.
A program may use at most 64 MiB of HBM per device.

```python
import math
import jax
import jax.numpy as jnp
import numpy as np
from jax import lax

D = 2048
F = 384
TOK_DEV = 128
COLD_DEV = 32
EXPERTS = 32
CAP = 2
ROWS = 131072
CROWS = 32768


def shard_levels(own_key, extent, pieces, least, largest):
    level = 1.0
    for axis_at, shards_of in pieces:
        steps = jax.random.uniform(jax.random.fold_in(jax.random.fold_in(own_key, 6), axis_at), (shards_of,), jnp.float32, least / len(pieces), largest / len(pieces))
        level = level * jnp.repeat(jnp.exp(steps), extent[axis_at] // shards_of).reshape((-1,) + (1,) * (len(extent) - 1 - axis_at))
    return level


def routed_block(own_key, own, number, rows, number_of, top, reach, slope):
    ranking = jax.random.permutation(own_key, number_of)
    crowded, common = load_shares(number_of, rows * top, reach, slope, True), load_shares(number_of, rows * top, reach, slope, False)
    places = jnp.arange(number_of)

    def named(tallies, turn):
        used = int((tallies > 0).sum())
        fixed = max(1, used // 4)
        moved = fixed + (places - fixed + turn * (used - fixed)) % max(1, number_of - fixed)
        return jnp.zeros((number_of,), jnp.int32).at[ranking[jnp.where(places < fixed, places, moved)]].set(jnp.asarray(tallies, jnp.int32))

    tallies = jnp.where(number % 4 == 0, named(crowded, number // 4), named(common, number - number // 4 - 1))
    mixed = jax.random.permutation(jax.random.fold_in(own, 3), number_of)
    donor, sink = mixed[0:number_of // 2 * 2:2], mixed[1:number_of // 2 * 2:2]
    room = jnp.minimum(tallies[donor] - 1, reach - tallies[sink]) // 2
    room = jnp.where((donor == ranking[0]) | (sink == ranking[0]) | (tallies[sink] == 0), 0, jnp.maximum(room, 0))
    moved = jax.random.randint(jax.random.fold_in(own, 4), (number_of // 2,), 0, 1 << 20) % (room + 1)
    tallies = tallies.at[donor].add(-moved).at[sink].add(moved)
    labels = jnp.searchsorted(jnp.cumsum(tallies), jnp.arange(rows * top), side="right").astype(jnp.int32)
    grid = labels.reshape(top, rows).T
    grid = grid[jax.random.permutation(jax.random.fold_in(own, 1), rows)]
    turn = jax.random.randint(jax.random.fold_in(own, 2), (rows, 1), 0, top)
    return jnp.take_along_axis(grid, (jnp.arange(top)[None, :] + turn) % top, axis=1)


def load_shares(count, total, limit, skew, full):
    weights = [(1 << 20) // math.isqrt(standing ** skew) + 1 for standing in range(1, count + 1)]
    largest = limit if full else min(limit, max(-(-total // count), total * weights[0] // sum(weights)))
    least = 1 if total - largest >= count - 1 else 0
    counts, spare = [largest] + [least] * (count - 1), total - largest - least * (count - 1)
    while spare > 0:
        candidates = [i for i in range(1, count) if counts[i] < largest] or [i for i in range(1, count) if counts[i] < limit]
        pool, remaining = sum([weights[i] for i in candidates]), spare
        for i in candidates:
            addition = min(limit - counts[i], max(1, remaining * weights[i] // pool), spare)
            counts[i] = counts[i] + addition
            spare = spare - addition
    return np.array(counts)


def gaussian(own_key, shape, width, bound, shards=(), kind=jnp.bfloat16):
    drawn = width * jax.random.normal(own_key, shape, jnp.float32)
    if shards:
        drawn = drawn * shard_levels(own_key, shape, shards, -0.22, 0.18)
    return jnp.clip(drawn, -bound, bound).astype(kind)


def setup_inputs(seed: int = 0) -> dict:
    arg_keys = jax.random.split(jax.random.key(seed), 9)
    tokens = gaussian(arg_keys[0], (ROWS, D), 1.0, 6.0, ((0, 1024),))
    hot_gate = jnp.clip(0.3 + 0.7 * jax.random.uniform(arg_keys[1], (ROWS,), jnp.float32) ** shard_levels(arg_keys[1], (ROWS,), ((0, 1024),), -0.2, 0.2), 0.3, 1.0)
    cold_expert_keys = jax.random.split(jax.random.fold_in(arg_keys[2], 1), CROWS // COLD_DEV)
    cold_expert_turns = jax.random.permutation(jax.random.fold_in(arg_keys[2], 3), CROWS // COLD_DEV)
    cold_expert = jax.vmap(lambda own, number: routed_block(jax.random.fold_in(arg_keys[2], 2), own, number, COLD_DEV, EXPERTS, 1, CAP, 2))(cold_expert_keys, cold_expert_turns).reshape((CROWS, 1))
    cold_gate = jnp.clip(0.3 + 0.7 * jax.random.uniform(arg_keys[3], (CROWS,), jnp.float32) ** shard_levels(arg_keys[3], (CROWS,), ((0, 1024),), -0.2, 0.2), 0.3, 1.0)
    hot_id = jax.random.randint(arg_keys[4], (1,), 0, 4096 * EXPERTS).astype(jnp.int32)
    w_gate = gaussian(arg_keys[5], (EXPERTS, D, F), D ** -0.5, 0.125, ((0, 32),))
    w_up = gaussian(arg_keys[6], (EXPERTS, D, F), D ** -0.5, 0.125, ((0, 32),))
    w_down = gaussian(arg_keys[7], (EXPERTS, F, D), F ** -0.5, 0.3125, ((0, 32),))
    return {"tokens": tokens, "hot_gate": hot_gate, "cold_expert": cold_expert, "cold_gate": cold_gate, "hot_id": hot_id, "w_gate": w_gate, "w_up": w_up, "w_down": w_down}


def expert_apply(inputs, gate_mat, up_mat, down_mat):
    gated = jnp.dot(inputs, gate_mat, preferred_element_type=jnp.float32)
    upper = jnp.dot(inputs, up_mat, preferred_element_type=jnp.float32)
    hidden = (jax.nn.silu(gated) * upper).astype(jnp.bfloat16)
    return jnp.dot(hidden, down_mat, preferred_element_type=jnp.float32)


def reference(tokens, hot_gate, cold_expert, cold_gate, hot_id, w_gate, w_up, w_down):
    blocks = ROWS // TOK_DEV
    grouped = tokens.reshape(blocks, TOK_DEV, D)
    cold_inputs = grouped[:, :COLD_DEV]
    target = cold_expert.reshape(blocks, COLD_DEV).astype(jnp.int32)
    onehot = (target[:, :, None] == jnp.arange(EXPERTS, dtype=jnp.int32)[None, None, :]).astype(jnp.int32)
    ranks_run = jnp.cumsum(onehot, axis=1)
    slot_of = (jnp.sum(ranks_run * onehot, axis=2) - 1).astype(jnp.int32)
    position = (target * CAP + slot_of).astype(jnp.int32)
    block_ids = jnp.broadcast_to(jnp.arange(blocks, dtype=jnp.int32)[:, None], (blocks, COLD_DEV))
    row_ids = jnp.broadcast_to(jnp.arange(COLD_DEV, dtype=jnp.int32)[None, :], (blocks, COLD_DEV))
    table = jnp.zeros((blocks, EXPERTS * CAP), jnp.int32).at[block_ids, position].set(row_ids)

    def per_expert(expert_num):
        chosen = lax.dynamic_slice_in_dim(table, expert_num * CAP, CAP, 1)
        gathered = cold_inputs[jnp.arange(blocks, dtype=jnp.int32)[:, None], chosen]
        result = expert_apply(gathered.reshape(blocks * CAP, D), w_gate[expert_num], w_up[expert_num], w_down[expert_num])
        return result.astype(jnp.bfloat16).reshape(blocks, CAP, D)

    served = lax.map(per_expert, jnp.arange(EXPERTS, dtype=jnp.int32))
    cold_out = served[target, block_ids, slot_of]

    owner = (hot_id[0] % EXPERTS).astype(jnp.int32)
    hot_g = w_gate[owner]
    hot_u = w_up[owner]
    hot_d = w_down[owner]
    gates_hot = hot_gate.reshape(blocks, TOK_DEV)
    gates_cold = cold_gate.reshape(blocks, COLD_DEV)

    def per_block(packed):
        inputs, weights_hot, returned, weights_cold = packed
        mixed = weights_hot[:, None] * expert_apply(inputs, hot_g, hot_u, hot_d)
        mixed = mixed.at[:COLD_DEV].add(weights_cold[:, None] * returned.astype(jnp.float32))
        return mixed.astype(jnp.bfloat16)

    output = lax.map(per_block, (grouped, gates_hot, cold_out, gates_cold))
    return output.reshape(ROWS, D)
```

```python
import jax
import jax.numpy as jnp
from jax import lax
from jax.sharding import PartitionSpec as P


def expert_apply(inputs, gate_mat, up_mat, down_mat):
    gated = jnp.dot(inputs, gate_mat, preferred_element_type=jnp.float32)
    upper = jnp.dot(inputs, up_mat, preferred_element_type=jnp.float32)
    hidden = (jax.nn.silu(gated) * upper).astype(jnp.bfloat16)
    return jnp.dot(hidden, down_mat, preferred_element_type=jnp.float32)


def hot_weights(w_gate, w_up, w_down, hot_id):
    groups = lax.axis_size("expert")
    replicas = lax.axis_size("dp")
    owner = hot_id[0] % groups
    share = w_gate.shape[2] // replicas
    offset = lax.axis_index("dp") * share
    piece_g = jnp.transpose(lax.dynamic_slice_in_dim(w_gate[0], offset, share, 1))
    piece_u = jnp.transpose(lax.dynamic_slice_in_dim(w_up[0], offset, share, 1))
    piece_d = lax.dynamic_slice_in_dim(w_down[0], offset, share, 0)
    piece = jnp.concatenate([piece_g, piece_u, piece_d], axis=1)
    mine = lax.axis_index("expert") == owner
    piece = jnp.where(mine, piece, jnp.zeros_like(piece))
    piece = lax.psum(piece, "expert")
    full = lax.all_gather(piece, "dp", axis=0, tiled=True)
    width = w_gate.shape[1]
    return full[:, :width], full[:, width:2 * width], full[:, 2 * width:]


def per_device(tokens, hot_gate, cold_expert, cold_gate, hot_id, w_gate, w_up, w_down):
    groups = lax.axis_size("expert")
    width = tokens.shape[1]
    dispatched = cold_expert.shape[0]
    capacity = max(2, 2 * dispatched // groups)

    hot_gt, hot_ut, hot_d = hot_weights(w_gate, w_up, w_down, hot_id)

    cold_inputs = tokens[:dispatched]
    target = cold_expert[:, 0]
    onehot = (target[:, None] == jnp.arange(groups, dtype=jnp.int32)[None, :]).astype(jnp.int32)
    ranks_run = jnp.cumsum(onehot, axis=0)
    slot_of = jnp.sum(ranks_run * onehot, axis=1) - 1
    position = target * capacity + slot_of
    outgoing = jnp.zeros((groups * capacity, width), jnp.bfloat16).at[position].set(cold_inputs)
    outgoing = outgoing.reshape(groups, capacity, width)
    received = lax.all_to_all(outgoing, "expert", split_axis=0, concat_axis=0, tiled=True)
    served = expert_apply(received.reshape(-1, width), w_gate[0], w_up[0], w_down[0]).astype(jnp.bfloat16)
    returned = lax.all_to_all(
        served.reshape(received.shape), "expert", split_axis=0, concat_axis=0, tiled=True
    )
    cold_out = returned.reshape(groups * capacity, width)[position].astype(jnp.float32)

    gated = lax.dot_general(tokens, hot_gt, (((1,), (1,)), ((), ())), preferred_element_type=jnp.float32)
    upper = lax.dot_general(tokens, hot_ut, (((1,), (1,)), ((), ())), preferred_element_type=jnp.float32)
    hidden = (jax.nn.silu(gated) * upper).astype(jnp.bfloat16)
    hot_out = jnp.dot(hidden, hot_d, preferred_element_type=jnp.float32)

    mixed = hot_gate[:, None] * hot_out
    mixed = mixed.at[:dispatched].add(cold_gate[:, None] * cold_out)
    return mixed.astype(jnp.bfloat16)


def solution(mesh):
    return jax.shard_map(
        per_device,
        mesh=mesh,
        in_specs=(
            P(("dp", "expert"), None),
            P(("dp", "expert")),
            P(("dp", "expert"), None),
            P(("dp", "expert")),
            P(),
            P("expert", None, None),
            P("expert", None, None),
            P("expert", None, None),
        ),
        out_specs=P(("dp", "expert"), None),
        check_vma=False,
    )
```

```python
import jax
import jax.numpy as jnp
from jax import lax
from jax.sharding import PartitionSpec as P


def expert_apply(inputs, gate_mat, up_mat, down_mat):
    gated = jnp.dot(inputs, gate_mat, preferred_element_type=jnp.float32)
    upper = jnp.dot(inputs, up_mat, preferred_element_type=jnp.float32)
    hidden = (jax.nn.silu(gated) * upper).astype(jnp.bfloat16)
    return jnp.dot(hidden, down_mat, preferred_element_type=jnp.float32)


def expert_bits(count):
    return count // 8, 4, 2


def hot_weights(w_gate, w_up, w_down, hot_id):
    groups = lax.axis_size("expert")
    replicas = lax.axis_size("dp")
    xs, zs, cores = expert_bits(groups)
    owner = hot_id[0] % groups
    share = w_gate.shape[2] // replicas
    half = share // cores
    offset = lax.axis_index("dp") * share
    piece_g = jnp.transpose(lax.dynamic_slice_in_dim(w_gate[0], offset, share, 1))
    piece_u = jnp.transpose(lax.dynamic_slice_in_dim(w_up[0], offset, share, 1))
    piece_d = lax.dynamic_slice_in_dim(w_down[0], offset, share, 0)
    piece = jnp.concatenate([piece_g, piece_u, piece_d], axis=1)
    me = lax.axis_index("expert")
    core = me % cores
    own_half = lax.dynamic_slice_in_dim(piece, core * half, half, 0)
    other_half = lax.dynamic_slice_in_dim(piece, (1 - core) * half, half, 0)

    swap = [(i, i ^ 1) for i in range(groups)]
    got = lax.ppermute(other_half, "expert", swap)
    have = jnp.where((me ^ 1) == owner, got, own_half)

    rel = me ^ owner
    known = 1
    for bit in (8, 16):
        pairs = [(i, i ^ bit) for i in range(groups)]
        got = lax.ppermute(have, "expert", pairs)
        take = (rel & ~known & ~6) == bit
        have = jnp.where(take, got, have)
        known |= bit

    def shifted(step):
        return [
            (i, (i & ~6) | ((((i >> 1) & 3) + step) % zs) << 1) for i in range(groups)
        ]

    distance = ((me >> 1) & 3) - ((owner >> 1) & 3)
    distance = distance % zs
    from_below = lax.ppermute(have, "expert", shifted(1))
    from_above = lax.ppermute(have, "expert", shifted(zs - 1))
    have = jnp.where(distance == 1, from_below, jnp.where(distance == zs - 1, from_above, have))
    from_below = lax.ppermute(have, "expert", shifted(1))
    have = jnp.where(distance == 2, from_below, have)

    mine = lax.all_gather(have, "dp", axis=0, tiled=True)
    theirs = lax.ppermute(mine, "expert", swap)
    full = jnp.concatenate([mine, theirs], axis=0)
    width = w_gate.shape[1]
    return full[:, :width], full[:, width:2 * width], full[:, 2 * width:]


def per_device(tokens, hot_gate, cold_expert, cold_gate, hot_id, w_gate, w_up, w_down):
    groups = lax.axis_size("expert")
    width = tokens.shape[1]
    dispatched = cold_expert.shape[0]
    capacity = max(2, 2 * dispatched // groups)

    hot_gt, hot_ut, hot_d = hot_weights(w_gate, w_up, w_down, hot_id)

    cold_inputs = tokens[:dispatched]
    target = cold_expert[:, 0]
    onehot = (target[:, None] == jnp.arange(groups, dtype=jnp.int32)[None, :]).astype(jnp.int32)
    ranks_run = jnp.cumsum(onehot, axis=0)
    slot_of = jnp.sum(ranks_run * onehot, axis=1) - 1
    position = target * capacity + slot_of
    outgoing = jnp.zeros((groups * capacity, width), jnp.bfloat16).at[position].set(cold_inputs)
    outgoing = outgoing.reshape(groups, capacity, width)
    received = lax.all_to_all(outgoing, "expert", split_axis=0, concat_axis=0, tiled=True)
    served = expert_apply(received.reshape(-1, width), w_gate[0], w_up[0], w_down[0]).astype(jnp.bfloat16)
    returned = lax.all_to_all(
        served.reshape(received.shape), "expert", split_axis=0, concat_axis=0, tiled=True
    )
    cold_out = returned.reshape(groups * capacity, width)[position].astype(jnp.float32)

    gated = lax.dot_general(tokens, hot_gt, (((1,), (1,)), ((), ())), preferred_element_type=jnp.float32)
    upper = lax.dot_general(tokens, hot_ut, (((1,), (1,)), ((), ())), preferred_element_type=jnp.float32)
    hidden = (jax.nn.silu(gated) * upper).astype(jnp.bfloat16)
    hot_out = jnp.dot(hidden, hot_d, preferred_element_type=jnp.float32)

    mixed = hot_gate[:, None] * hot_out
    mixed = mixed.at[:dispatched].add(cold_gate[:, None] * cold_out)
    return mixed.astype(jnp.bfloat16)


def solution(mesh):
    return jax.shard_map(
        per_device,
        mesh=mesh,
        in_specs=(
            P(("dp", "expert"), None),
            P(("dp", "expert")),
            P(("dp", "expert"), None),
            P(("dp", "expert")),
            P(),
            P("expert", None, None),
            P("expert", None, None),
            P("expert", None, None),
        ),
        out_specs=P(("dp", "expert"), None),
        check_vma=False,
    )
```

```python
import jax
import jax.numpy as jnp
from jax import lax
from jax.sharding import PartitionSpec as P


def expert_apply(inputs, gate_mat, up_mat, down_mat):
    gated = jnp.dot(inputs, gate_mat, preferred_element_type=jnp.float32)
    upper = jnp.dot(inputs, up_mat, preferred_element_type=jnp.float32)
    hidden = (jax.nn.silu(gated) * upper).astype(jnp.bfloat16)
    return jnp.dot(hidden, down_mat, preferred_element_type=jnp.float32)


def expert_bits(count):
    return count // 8, 4, 2


def y_shift(step):
    replicas = 32
    return [(d, (d // 4) * 4 + (d % 4 + step) % 4) for d in range(replicas)]


def z_shift(step):
    pairs = []
    for d in range(32):
        for e in range(32):
            z = ((e >> 1) & 3) * 8 + d // 4
            moved = (z + step) % 32
            pairs.append((d * 32 + e, ((moved % 8) * 4 + d % 4) * 32 + ((e & ~6) | ((moved // 8) << 1))))
    return pairs


def gather_over_dp(have):
    up = lax.ppermute(have, "dp", y_shift(1))
    down = lax.ppermute(have, "dp", y_shift(-1))
    up2 = lax.ppermute(up, "dp", y_shift(1))
    bundle = jnp.concatenate([have, up, down, up2], axis=0)
    axes = ("dp", "expert")
    parts = [bundle]
    below = bundle
    above = bundle
    for step in range(4):
        below = lax.ppermute(below, axes, z_shift(1))
        parts.append(below)
        if step < 3:
            above = lax.ppermute(above, axes, z_shift(-1))
            parts.append(above)
    return jnp.concatenate(parts, axis=0)


def x_shift(step):
    return [(i, (i & 7) | ((((i >> 3) + step) % 4) << 3)) for i in range(32)]


def arranged(g, u, d, pieces):
    rows, width = g.shape
    cols = width // pieces
    stacked = jnp.stack([m.reshape(rows, pieces, cols) for m in (g, u, d)], axis=2)
    return stacked.reshape(rows, pieces * 3 * cols)


def hot_weights(w_gate, w_up, w_down, hot_id):
    groups = lax.axis_size("expert")
    replicas = lax.axis_size("dp")
    xs, zs, cores = expert_bits(groups)
    owner = hot_id[0] % groups
    share = w_gate.shape[2] // replicas
    half = share // cores
    me = lax.axis_index("expert")
    core = me % cores
    xpos = me >> 3
    base = lax.axis_index("dp") * share

    def rows_of(c):
        start = base + c * half
        g = jnp.transpose(lax.dynamic_slice_in_dim(w_gate[0], start, half, 1))
        u = jnp.transpose(lax.dynamic_slice_in_dim(w_up[0], start, half, 1))
        d = lax.dynamic_slice_in_dim(w_down[0], start, half, 0)
        return arranged(g, u, d, xs)

    own_half = rows_of(core)
    other_half = rows_of(1 - core)
    swap = [(i, i ^ 1) for i in range(groups)]
    got = lax.ppermute(other_half, "expert", swap)
    have = jnp.where((me ^ 1) == owner, got, own_half)

    rel = me ^ owner
    piece = have.shape[1] // xs
    pair = lax.dynamic_slice_in_dim(have, ((xpos >> 1) ^ 1) * 2 * piece, 2 * piece, 1)
    got = lax.ppermute(pair, "expert", [(i, i ^ 16) for i in range(groups)])
    mine_pair = lax.dynamic_slice_in_dim(have, (xpos >> 1) * 2 * piece, 2 * piece, 1)
    have = jnp.where((rel & 16) != 0, got, mine_pair)
    one = lax.dynamic_slice_in_dim(have, ((xpos ^ 1) & 1) * piece, piece, 1)
    got = lax.ppermute(one, "expert", [(i, i ^ 8) for i in range(groups)])
    mine_one = lax.dynamic_slice_in_dim(have, (xpos & 1) * piece, piece, 1)
    have = jnp.where((rel & 8) != 0, got, mine_one)

    def shifted(step):
        return [
            (i, (i & ~6) | ((((i >> 1) & 3) + step) % zs) << 1) for i in range(groups)
        ]

    distance = ((me >> 1) & 3) - ((owner >> 1) & 3)
    distance = distance % zs
    from_below = lax.ppermute(have, "expert", shifted(1))
    from_above = lax.ppermute(have, "expert", shifted(zs - 1))
    have = jnp.where(distance == 1, from_below, jnp.where(distance == zs - 1, from_above, have))
    from_below = lax.ppermute(have, "expert", shifted(1))
    have = jnp.where(distance == 2, from_below, have)

    mine = gather_over_dp(have)
    left = lax.ppermute(mine, "expert", x_shift(1))
    right = lax.ppermute(mine, "expert", x_shift(-1))
    left2 = lax.ppermute(left, "expert", x_shift(1))
    held = [mine, left, right, left2]
    which = [(xpos + k) % xs for k in (0, -1, 1, -2)]
    theirs = [lax.ppermute(p, "expert", swap) for p in held]
    return held, theirs, which


def per_device(tokens, hot_gate, cold_expert, cold_gate, hot_id, w_gate, w_up, w_down):
    groups = lax.axis_size("expert")
    width = tokens.shape[1]
    dispatched = cold_expert.shape[0]
    capacity = max(2, 2 * dispatched // groups)

    held, theirs, which = hot_weights(w_gate, w_up, w_down, hot_id)

    cold_inputs = tokens[:dispatched]
    target = cold_expert[:, 0]
    onehot = (target[:, None] == jnp.arange(groups, dtype=jnp.int32)[None, :]).astype(jnp.int32)
    ranks_run = jnp.cumsum(onehot, axis=0)
    slot_of = jnp.sum(ranks_run * onehot, axis=1) - 1
    position = target * capacity + slot_of
    outgoing = jnp.zeros((groups * capacity, width), jnp.bfloat16).at[position].set(cold_inputs)
    outgoing = outgoing.reshape(groups, capacity, width)
    received = lax.all_to_all(outgoing, "expert", split_axis=0, concat_axis=0, tiled=True)
    served = expert_apply(received.reshape(-1, width), w_gate[0], w_up[0], w_down[0]).astype(jnp.bfloat16)
    returned = lax.all_to_all(
        served.reshape(received.shape), "expert", split_axis=0, concat_axis=0, tiled=True
    )
    cold_out = returned.reshape(groups * capacity, width)[position].astype(jnp.float32)

    cols = width // len(which)
    token_parts = [lax.dynamic_slice_in_dim(tokens, q * cols, cols, 1) for q in which]
    contract = (((1,), (1,)), ((), ()))
    outs = [None] * len(which)
    for rows in (held, theirs):
        gated = None
        upper = None
        for part, tok in zip(rows, token_parts):
            g = lax.dot_general(tok, part[:, :cols], contract, preferred_element_type=jnp.float32)
            u = lax.dot_general(tok, part[:, cols:2 * cols], contract, preferred_element_type=jnp.float32)
            gated = g if gated is None else gated + g
            upper = u if upper is None else upper + u
        hidden = (jax.nn.silu(gated) * upper).astype(jnp.bfloat16)
        for k, part in enumerate(rows):
            o = jnp.dot(hidden, part[:, 2 * cols:], preferred_element_type=jnp.float32)
            outs[k] = o if outs[k] is None else outs[k] + o
    hot_out = jnp.zeros((tokens.shape[0], width), jnp.float32)
    for q, o in zip(which, outs):
        hot_out = lax.dynamic_update_slice_in_dim(hot_out, o, q * cols, 1)

    mixed = hot_gate[:, None] * hot_out
    mixed = mixed.at[:dispatched].add(cold_gate[:, None] * cold_out)
    return mixed.astype(jnp.bfloat16)


def solution(mesh):
    return jax.shard_map(
        per_device,
        mesh=mesh,
        in_specs=(
            P(("dp", "expert"), None),
            P(("dp", "expert")),
            P(("dp", "expert"), None),
            P(("dp", "expert")),
            P(),
            P("expert", None, None),
            P("expert", None, None),
            P("expert", None, None),
        ),
        out_specs=P(("dp", "expert"), None),
        check_vma=False,
    )
```

```python
import jax
import jax.numpy as jnp
from jax import lax
from jax.sharding import PartitionSpec as P


def expert_apply(inputs, gate_mat, up_mat, down_mat):
    gated = jnp.dot(inputs, gate_mat, preferred_element_type=jnp.float32)
    upper = jnp.dot(inputs, up_mat, preferred_element_type=jnp.float32)
    hidden = (jax.nn.silu(gated) * upper).astype(jnp.bfloat16)
    return jnp.dot(hidden, down_mat, preferred_element_type=jnp.float32)


def expert_bits(count):
    return count // 8, 4, 2


def y_shift(step):
    replicas = 32
    return [(d, (d // 4) * 4 + (d % 4 + step) % 4) for d in range(replicas)]


def z_shift(step):
    pairs = []
    for d in range(32):
        for e in range(32):
            z = ((e >> 1) & 3) * 8 + d // 4
            moved = (z + step) % 32
            pairs.append((d * 32 + e, ((moved % 8) * 4 + d % 4) * 32 + ((e & ~6) | ((moved // 8) << 1))))
    return pairs


def gather_over_dp(have):
    up = lax.ppermute(have, "dp", y_shift(1))
    down = lax.ppermute(have, "dp", y_shift(-1))
    up2 = lax.ppermute(up, "dp", y_shift(1))
    bundle = jnp.concatenate([have, up, down, up2], axis=0)
    axes = ("dp", "expert")
    parts = [bundle]
    below = bundle
    above = bundle
    for step in range(4):
        below = lax.ppermute(below, axes, z_shift(1))
        parts.append(below)
        if step < 3:
            above = lax.ppermute(above, axes, z_shift(-1))
            parts.append(above)
    return jnp.concatenate(parts, axis=0)


def x_shift(step):
    return [(i, (i & 7) | ((((i >> 3) + step) % 4) << 3)) for i in range(32)]


def arranged(g, u, d, pieces):
    rows, width = g.shape
    cols = width // pieces
    stacked = jnp.stack([m.reshape(rows, pieces, cols) for m in (g, u, d)], axis=2)
    return stacked.reshape(rows, pieces * 3 * cols)


def hot_weights(w_gate, w_up, w_down, hot_id, early, late):
    groups = lax.axis_size("expert")
    replicas = lax.axis_size("dp")
    xs, zs, cores = expert_bits(groups)
    owner = hot_id[0] % groups
    share = w_gate.shape[2] // replicas
    half = share // cores
    me = lax.axis_index("expert")
    core = me % cores
    xpos = me >> 3
    base = lax.axis_index("dp") * share

    def rows_of(c):
        start = base + c * half
        g = jnp.transpose(lax.dynamic_slice_in_dim(w_gate[0], start, half, 1))
        u = jnp.transpose(lax.dynamic_slice_in_dim(w_up[0], start, half, 1))
        d = lax.dynamic_slice_in_dim(w_down[0], start, half, 0)
        return arranged(g, u, d, xs)

    own_half = rows_of(core)
    other_half = rows_of(1 - core)
    swap = [(i, i ^ 1) for i in range(groups)]
    got = lax.ppermute(other_half, "expert", swap)
    have = jnp.where((me ^ 1) == owner, got, own_half)

    rel = me ^ owner
    piece = have.shape[1] // xs
    pair = lax.dynamic_slice_in_dim(have, ((xpos >> 1) ^ 1) * 2 * piece, 2 * piece, 1)
    got = lax.ppermute(pair, "expert", [(i, i ^ 16) for i in range(groups)])
    mine_pair = lax.dynamic_slice_in_dim(have, (xpos >> 1) * 2 * piece, 2 * piece, 1)
    have = jnp.where((rel & 16) != 0, got, mine_pair)
    one = lax.dynamic_slice_in_dim(have, ((xpos ^ 1) & 1) * piece, piece, 1)
    got = lax.ppermute(one, "expert", [(i, i ^ 8) for i in range(groups)])
    mine_one = lax.dynamic_slice_in_dim(have, (xpos & 1) * piece, piece, 1)
    have = jnp.where((rel & 8) != 0, got, mine_one)

    have = early(have)

    def shifted(step):
        return [
            (i, (i & ~6) | ((((i >> 1) & 3) + step) % zs) << 1) for i in range(groups)
        ]

    distance = ((me >> 1) & 3) - ((owner >> 1) & 3)
    distance = distance % zs
    from_below = lax.ppermute(have, "expert", shifted(1))
    from_above = lax.ppermute(have, "expert", shifted(zs - 1))
    have = jnp.where(distance == 1, from_below, jnp.where(distance == zs - 1, from_above, have))
    from_below = lax.ppermute(have, "expert", shifted(1))
    have = jnp.where(distance == 2, from_below, have)

    mine = late(gather_over_dp(have))
    left = lax.ppermute(mine, "expert", x_shift(1))
    right = lax.ppermute(mine, "expert", x_shift(-1))
    left2 = lax.ppermute(left, "expert", x_shift(1))
    held = [mine, left, right, left2]
    which = [(xpos + k) % xs for k in (0, -1, 1, -2)]
    theirs = [lax.ppermute(p, "expert", swap) for p in held]
    return held, theirs, which


def per_device(tokens, hot_gate, cold_expert, cold_gate, hot_id, w_gate, w_up, w_down):
    groups = lax.axis_size("expert")
    width = tokens.shape[1]
    dispatched = cold_expert.shape[0]
    capacity = max(2, 2 * dispatched // groups)

    cold_inputs = tokens[:dispatched]
    target = cold_expert[:, 0]
    onehot = (target[:, None] == jnp.arange(groups, dtype=jnp.int32)[None, :]).astype(jnp.int32)
    ranks_run = jnp.cumsum(onehot, axis=0)
    slot_of = jnp.sum(ranks_run * onehot, axis=1) - 1
    position = target * capacity + slot_of
    outgoing = jnp.zeros((groups * capacity, width), jnp.bfloat16).at[position].set(cold_inputs)
    outgoing = outgoing.reshape(groups, capacity, width)
    received = lax.all_to_all(outgoing, "expert", split_axis=0, concat_axis=0, tiled=True)
    cold = {}

    def early(have):
        arrived, have = lax.optimization_barrier((received, have))
        served = expert_apply(arrived.reshape(-1, width), w_gate[0], w_up[0], w_down[0]).astype(jnp.bfloat16)
        cold["back"] = lax.all_to_all(
            served.reshape(arrived.shape), "expert", split_axis=0, concat_axis=0, tiled=True
        )
        return have

    def late(mine):
        back, mine = lax.optimization_barrier((cold["back"], mine))
        cold["out"] = back.reshape(groups * capacity, width)[position].astype(jnp.float32)
        return mine

    held, theirs, which = hot_weights(w_gate, w_up, w_down, hot_id, early, late)
    cold_out = cold["out"]


    cols = width // len(which)
    token_parts = [lax.dynamic_slice_in_dim(tokens, q * cols, cols, 1) for q in which]
    contract = (((1,), (1,)), ((), ()))
    outs = [None] * len(which)
    for rows in (held, theirs):
        gated = None
        upper = None
        for part, tok in zip(rows, token_parts):
            g = lax.dot_general(tok, part[:, :cols], contract, preferred_element_type=jnp.float32)
            u = lax.dot_general(tok, part[:, cols:2 * cols], contract, preferred_element_type=jnp.float32)
            gated = g if gated is None else gated + g
            upper = u if upper is None else upper + u
        hidden = (jax.nn.silu(gated) * upper).astype(jnp.bfloat16)
        for k, part in enumerate(rows):
            o = jnp.dot(hidden, part[:, 2 * cols:], preferred_element_type=jnp.float32)
            outs[k] = o if outs[k] is None else outs[k] + o
    hot_out = jnp.zeros((tokens.shape[0], width), jnp.float32)
    for q, o in zip(which, outs):
        hot_out = lax.dynamic_update_slice_in_dim(hot_out, o, q * cols, 1)

    mixed = hot_gate[:, None] * hot_out
    mixed = mixed.at[:dispatched].add(cold_gate[:, None] * cold_out)
    return mixed.astype(jnp.bfloat16)


def solution(mesh):
    return jax.shard_map(
        per_device,
        mesh=mesh,
        in_specs=(
            P(("dp", "expert"), None),
            P(("dp", "expert")),
            P(("dp", "expert"), None),
            P(("dp", "expert")),
            P(),
            P("expert", None, None),
            P("expert", None, None),
            P("expert", None, None),
        ),
        out_specs=P(("dp", "expert"), None),
        check_vma=False,
    )
```

```python
import jax
import jax.numpy as jnp
from jax import lax
from jax.sharding import PartitionSpec as P


def expert_apply(inputs, gate_mat, up_mat, down_mat):
    gated = jnp.dot(inputs, gate_mat, preferred_element_type=jnp.float32)
    upper = jnp.dot(inputs, up_mat, preferred_element_type=jnp.float32)
    hidden = (jax.nn.silu(gated) * upper).astype(jnp.bfloat16)
    return jnp.dot(hidden, down_mat, preferred_element_type=jnp.float32)


def expert_bits(count):
    return count // 8, 4, 2


def y_shift(step):
    replicas = 32
    return [(d, (d // 4) * 4 + (d % 4 + step) % 4) for d in range(replicas)]


def z_shift(step):
    pairs = []
    for d in range(32):
        for e in range(32):
            z = ((e >> 1) & 3) * 8 + d // 4
            moved = (z + step) % 32
            pairs.append((d * 32 + e, ((moved % 8) * 4 + d % 4) * 32 + ((e & ~6) | ((moved // 8) << 1))))
    return pairs


def gather_over_dp(have):
    up = lax.ppermute(have, "dp", y_shift(1))
    down = lax.ppermute(have, "dp", y_shift(-1))
    up2 = lax.ppermute(up, "dp", y_shift(1))
    bundle = jnp.concatenate([have, up, down, up2], axis=0)
    axes = ("dp", "expert")
    parts = [bundle]
    below = bundle
    above = bundle
    for step in range(4):
        below = lax.ppermute(below, axes, z_shift(1))
        parts.append(below)
        if step < 3:
            above = lax.ppermute(above, axes, z_shift(-1))
            parts.append(above)
    return jnp.concatenate(parts, axis=0)


def x_shift(step):
    return [(i, (i & 7) | ((((i >> 3) + step) % 4) << 3)) for i in range(32)]


def arranged(g, u, d, pieces):
    rows, width = g.shape
    cols = width // pieces
    stacked = jnp.stack([m.reshape(rows, pieces, cols) for m in (g, u, d)], axis=2)
    return stacked.reshape(rows, pieces * 3 * cols)


def hot_weights(w_gate, w_up, w_down, hot_id, early, middle, late):
    groups = lax.axis_size("expert")
    replicas = lax.axis_size("dp")
    xs, zs, cores = expert_bits(groups)
    owner = hot_id[0] % groups
    share = w_gate.shape[2] // replicas
    half = share // cores
    me = lax.axis_index("expert")
    core = me % cores
    xpos = me >> 3
    base = lax.axis_index("dp") * share

    def rows_of(c):
        start = base + c * half
        g = jnp.transpose(lax.dynamic_slice_in_dim(w_gate[0], start, half, 1))
        u = jnp.transpose(lax.dynamic_slice_in_dim(w_up[0], start, half, 1))
        d = lax.dynamic_slice_in_dim(w_down[0], start, half, 0)
        return arranged(g, u, d, xs)

    own_half = rows_of(core)
    other_half = rows_of(1 - core)
    swap = [(i, i ^ 1) for i in range(groups)]
    got = lax.ppermute(other_half, "expert", swap)
    have = jnp.where((me ^ 1) == owner, got, own_half)

    rel = me ^ owner
    piece = have.shape[1] // xs
    pair = lax.dynamic_slice_in_dim(have, ((xpos >> 1) ^ 1) * 2 * piece, 2 * piece, 1)
    got = lax.ppermute(pair, "expert", [(i, i ^ 16) for i in range(groups)])
    mine_pair = lax.dynamic_slice_in_dim(have, (xpos >> 1) * 2 * piece, 2 * piece, 1)
    have = jnp.where((rel & 16) != 0, got, mine_pair)
    one = lax.dynamic_slice_in_dim(have, ((xpos ^ 1) & 1) * piece, piece, 1)
    got = lax.ppermute(one, "expert", [(i, i ^ 8) for i in range(groups)])
    mine_one = lax.dynamic_slice_in_dim(have, (xpos & 1) * piece, piece, 1)
    have = jnp.where((rel & 8) != 0, got, mine_one)

    have = early(have)

    def shifted(step):
        return [
            (i, (i & ~6) | ((((i >> 1) & 3) + step) % zs) << 1) for i in range(groups)
        ]

    distance = ((me >> 1) & 3) - ((owner >> 1) & 3)
    distance = distance % zs
    from_below = lax.ppermute(have, "expert", shifted(1))
    from_above = lax.ppermute(have, "expert", shifted(zs - 1))
    from_far = lax.ppermute(have, "expert", shifted(2))
    have = jnp.where(
        distance == 1, from_below, jnp.where(distance == zs - 1, from_above, jnp.where(distance == 2, from_far, have))
    )
    have = middle(have)

    mine = late(gather_over_dp(have))
    left = lax.ppermute(mine, "expert", x_shift(1))
    right = lax.ppermute(mine, "expert", x_shift(-1))
    left2 = lax.ppermute(left, "expert", x_shift(1))
    held = [mine, left, right, left2]
    which = [(xpos + k) % xs for k in (0, -1, 1, -2)]
    theirs = [lax.ppermute(p, "expert", swap) for p in held]
    return held, theirs, which


def per_device(tokens, hot_gate, cold_expert, cold_gate, hot_id, w_gate, w_up, w_down):
    groups = lax.axis_size("expert")
    width = tokens.shape[1]
    dispatched = cold_expert.shape[0]
    capacity = max(2, 2 * dispatched // groups)

    cold_inputs = tokens[:dispatched]
    target = cold_expert[:, 0]
    onehot = (target[:, None] == jnp.arange(groups, dtype=jnp.int32)[None, :]).astype(jnp.int32)
    ranks_run = jnp.cumsum(onehot, axis=0)
    slot_of = jnp.sum(ranks_run * onehot, axis=1) - 1
    position = target * capacity + slot_of
    outgoing = jnp.zeros((groups * capacity, width), jnp.bfloat16).at[position].set(cold_inputs)
    outgoing = outgoing.reshape(groups, capacity, width)
    received = lax.all_to_all(outgoing, "expert", split_axis=0, concat_axis=0, tiled=True)
    cold = {}

    def early(have):
        arrived, have = lax.optimization_barrier((received, have))
        cold["served"] = expert_apply(arrived.reshape(-1, width), w_gate[0], w_up[0], w_down[0]).astype(jnp.bfloat16)
        return have

    def middle(have):
        served, have = lax.optimization_barrier((cold["served"], have))
        cold["back"] = lax.all_to_all(
            served.reshape(received.shape), "expert", split_axis=0, concat_axis=0, tiled=True
        )
        return have

    def late(mine):
        back, mine = lax.optimization_barrier((cold["back"], mine))
        cold["out"] = back.reshape(groups * capacity, width)[position].astype(jnp.float32)
        return mine

    held, theirs, which = hot_weights(w_gate, w_up, w_down, hot_id, early, middle, late)
    cold_out = cold["out"]


    cols = width // len(which)
    token_parts = [lax.dynamic_slice_in_dim(tokens, q * cols, cols, 1) for q in which]
    contract = (((1,), (1,)), ((), ()))
    outs = [None] * len(which)
    for rows in (held, theirs):
        gated = None
        upper = None
        for part, tok in zip(rows, token_parts):
            g = lax.dot_general(tok, part[:, :cols], contract, preferred_element_type=jnp.float32)
            u = lax.dot_general(tok, part[:, cols:2 * cols], contract, preferred_element_type=jnp.float32)
            gated = g if gated is None else gated + g
            upper = u if upper is None else upper + u
        hidden = (jax.nn.silu(gated) * upper).astype(jnp.bfloat16)
        for k, part in enumerate(rows):
            o = jnp.dot(hidden, part[:, 2 * cols:], preferred_element_type=jnp.float32)
            outs[k] = o if outs[k] is None else outs[k] + o
    hot_out = jnp.zeros((tokens.shape[0], width), jnp.float32)
    for q, o in zip(which, outs):
        hot_out = lax.dynamic_update_slice_in_dim(hot_out, o, q * cols, 1)

    mixed = hot_gate[:, None] * hot_out
    mixed = mixed.at[:dispatched].add(cold_gate[:, None] * cold_out)
    return mixed.astype(jnp.bfloat16)


def solution(mesh):
    return jax.shard_map(
        per_device,
        mesh=mesh,
        in_specs=(
            P(("dp", "expert"), None),
            P(("dp", "expert")),
            P(("dp", "expert"), None),
            P(("dp", "expert")),
            P(),
            P("expert", None, None),
            P("expert", None, None),
            P("expert", None, None),
        ),
        out_specs=P(("dp", "expert"), None),
        check_vma=False,
    )
```

```python
import jax
import jax.numpy as jnp
from jax import lax
from jax.sharding import PartitionSpec as P


def expert_apply(inputs, gate_mat, up_mat, down_mat):
    gated = jnp.dot(inputs, gate_mat, preferred_element_type=jnp.float32)
    upper = jnp.dot(inputs, up_mat, preferred_element_type=jnp.float32)
    hidden = (jax.nn.silu(gated) * upper).astype(jnp.bfloat16)
    return jnp.dot(hidden, down_mat, preferred_element_type=jnp.float32)


def expert_bits(count):
    return count // 8, 4, 2


def y_shift(step):
    replicas = 32
    return [(d, (d // 4) * 4 + (d % 4 + step) % 4) for d in range(replicas)]


def z_shift(step):
    pairs = []
    for d in range(32):
        for e in range(32):
            z = ((e >> 1) & 3) * 8 + d // 4
            moved = (z + step) % 32
            pairs.append((d * 32 + e, ((moved % 8) * 4 + d % 4) * 32 + ((e & ~6) | ((moved // 8) << 1))))
    return pairs


def gather_over_dp(have):
    up = lax.ppermute(have, "dp", y_shift(1))
    down = lax.ppermute(have, "dp", y_shift(-1))
    up2 = lax.ppermute(up, "dp", y_shift(1))
    bundle = jnp.concatenate([have, up, down, up2], axis=0)
    axes = ("dp", "expert")
    below = lax.ppermute(bundle, axes, z_shift(1))
    above = lax.ppermute(bundle, axes, z_shift(-1))
    parts = [bundle, below, above]
    parts += [lax.ppermute(p, axes, z_shift(3)) for p in (bundle, below, above)]
    parts += [lax.ppermute(p, axes, z_shift(-3)) for p in (bundle, below)]
    return jnp.concatenate(parts, axis=0)


def x_shift(step):
    return [(i, (i & 7) | ((((i >> 3) + step) % 4) << 3)) for i in range(32)]


def arranged(g, u, d, pieces):
    rows, width = g.shape
    cols = width // pieces
    stacked = jnp.stack([m.reshape(rows, pieces, cols) for m in (g, u, d)], axis=2)
    return stacked.reshape(rows, pieces * 3 * cols)


def hot_weights(w_gate, w_up, w_down, hot_id, early, middle, late):
    groups = lax.axis_size("expert")
    replicas = lax.axis_size("dp")
    xs, zs, cores = expert_bits(groups)
    owner = hot_id[0] % groups
    share = w_gate.shape[2] // replicas
    half = share // cores
    me = lax.axis_index("expert")
    core = me % cores
    xpos = me >> 3
    base = lax.axis_index("dp") * share

    def rows_of(c):
        start = base + c * half
        g = jnp.transpose(lax.dynamic_slice_in_dim(w_gate[0], start, half, 1))
        u = jnp.transpose(lax.dynamic_slice_in_dim(w_up[0], start, half, 1))
        d = lax.dynamic_slice_in_dim(w_down[0], start, half, 0)
        return arranged(g, u, d, xs)

    own_half = rows_of(core)
    other_half = rows_of(1 - core)
    swap = [(i, i ^ 1) for i in range(groups)]
    got = lax.ppermute(other_half, "expert", swap)
    have = jnp.where((me ^ 1) == owner, got, own_half)

    rel = me ^ owner
    piece = have.shape[1] // xs
    pair = lax.dynamic_slice_in_dim(have, ((xpos >> 1) ^ 1) * 2 * piece, 2 * piece, 1)
    got = lax.ppermute(pair, "expert", [(i, i ^ 16) for i in range(groups)])
    mine_pair = lax.dynamic_slice_in_dim(have, (xpos >> 1) * 2 * piece, 2 * piece, 1)
    have = jnp.where((rel & 16) != 0, got, mine_pair)
    one = lax.dynamic_slice_in_dim(have, ((xpos ^ 1) & 1) * piece, piece, 1)
    got = lax.ppermute(one, "expert", [(i, i ^ 8) for i in range(groups)])
    mine_one = lax.dynamic_slice_in_dim(have, (xpos & 1) * piece, piece, 1)
    have = jnp.where((rel & 8) != 0, got, mine_one)

    have = early(have)

    def shifted(step):
        return [
            (i, (i & ~6) | ((((i >> 1) & 3) + step) % zs) << 1) for i in range(groups)
        ]

    distance = ((me >> 1) & 3) - ((owner >> 1) & 3)
    distance = distance % zs
    from_below = lax.ppermute(have, "expert", shifted(1))
    from_above = lax.ppermute(have, "expert", shifted(zs - 1))
    from_far = lax.ppermute(have, "expert", shifted(2))
    have = jnp.where(
        distance == 1, from_below, jnp.where(distance == zs - 1, from_above, jnp.where(distance == 2, from_far, have))
    )
    have = middle(have)

    mine = late(gather_over_dp(have))
    left = lax.ppermute(mine, "expert", x_shift(1))
    right = lax.ppermute(mine, "expert", x_shift(-1))
    left2 = lax.ppermute(left, "expert", x_shift(1))
    held = [mine, left, right, left2]
    which = [(xpos + k) % xs for k in (0, -1, 1, -2)]
    theirs = [lax.ppermute(p, "expert", swap) for p in held]
    return held, theirs, which


def per_device(tokens, hot_gate, cold_expert, cold_gate, hot_id, w_gate, w_up, w_down):
    groups = lax.axis_size("expert")
    width = tokens.shape[1]
    dispatched = cold_expert.shape[0]
    capacity = max(2, 2 * dispatched // groups)

    cold_inputs = tokens[:dispatched]
    target = cold_expert[:, 0]
    onehot = (target[:, None] == jnp.arange(groups, dtype=jnp.int32)[None, :]).astype(jnp.int32)
    ranks_run = jnp.cumsum(onehot, axis=0)
    slot_of = jnp.sum(ranks_run * onehot, axis=1) - 1
    position = target * capacity + slot_of
    outgoing = jnp.zeros((groups * capacity, width), jnp.bfloat16).at[position].set(cold_inputs)
    outgoing = outgoing.reshape(groups, capacity, width)
    received = lax.all_to_all(outgoing, "expert", split_axis=0, concat_axis=0, tiled=True)
    cold = {}

    def early(have):
        arrived, have = lax.optimization_barrier((received, have))
        cold["served"] = expert_apply(arrived.reshape(-1, width), w_gate[0], w_up[0], w_down[0]).astype(jnp.bfloat16)
        return have

    def middle(have):
        served, have = lax.optimization_barrier((cold["served"], have))
        cold["back"] = lax.all_to_all(
            served.reshape(received.shape), "expert", split_axis=0, concat_axis=0, tiled=True
        )
        return have

    def late(mine):
        back, mine = lax.optimization_barrier((cold["back"], mine))
        cold["out"] = back.reshape(groups * capacity, width)[position].astype(jnp.float32)
        return mine

    held, theirs, which = hot_weights(w_gate, w_up, w_down, hot_id, early, middle, late)
    cold_out = cold["out"]


    cols = width // len(which)
    token_parts = [lax.dynamic_slice_in_dim(tokens, q * cols, cols, 1) for q in which]
    contract = (((1,), (1,)), ((), ()))
    outs = [None] * len(which)
    for rows in (held, theirs):
        gated = None
        upper = None
        for part, tok in zip(rows, token_parts):
            g = lax.dot_general(tok, part[:, :cols], contract, preferred_element_type=jnp.float32)
            u = lax.dot_general(tok, part[:, cols:2 * cols], contract, preferred_element_type=jnp.float32)
            gated = g if gated is None else gated + g
            upper = u if upper is None else upper + u
        hidden = (jax.nn.silu(gated) * upper).astype(jnp.bfloat16)
        for k, part in enumerate(rows):
            o = jnp.dot(hidden, part[:, 2 * cols:], preferred_element_type=jnp.float32)
            outs[k] = o if outs[k] is None else outs[k] + o
    hot_out = jnp.zeros((tokens.shape[0], width), jnp.float32)
    for q, o in zip(which, outs):
        hot_out = lax.dynamic_update_slice_in_dim(hot_out, o, q * cols, 1)

    mixed = hot_gate[:, None] * hot_out
    mixed = mixed.at[:dispatched].add(cold_gate[:, None] * cold_out)
    return mixed.astype(jnp.bfloat16)


def solution(mesh):
    return jax.shard_map(
        per_device,
        mesh=mesh,
        in_specs=(
            P(("dp", "expert"), None),
            P(("dp", "expert")),
            P(("dp", "expert"), None),
            P(("dp", "expert")),
            P(),
            P("expert", None, None),
            P("expert", None, None),
            P("expert", None, None),
        ),
        out_specs=P(("dp", "expert"), None),
        check_vma=False,
    )
```

```python
import jax
import jax.numpy as jnp
from jax import lax
from jax.sharding import PartitionSpec as P


def expert_apply(inputs, gate_mat, up_mat, down_mat):
    gated = jnp.dot(inputs, gate_mat, preferred_element_type=jnp.float32)
    upper = jnp.dot(inputs, up_mat, preferred_element_type=jnp.float32)
    hidden = (jax.nn.silu(gated) * upper).astype(jnp.bfloat16)
    return jnp.dot(hidden, down_mat, preferred_element_type=jnp.float32)


def expert_bits(count):
    return count // 8, 4, 2


def y_shift(step):
    replicas = 32
    return [(d, (d // 4) * 4 + (d % 4 + step) % 4) for d in range(replicas)]


def z_shift(step):
    pairs = []
    for d in range(32):
        for e in range(32):
            z = ((e >> 1) & 3) * 8 + d // 4
            moved = (z + step) % 32
            pairs.append((d * 32 + e, ((moved % 8) * 4 + d % 4) * 32 + ((e & ~6) | ((moved // 8) << 1))))
    return pairs


def gather_over_dp(have):
    up = lax.ppermute(have, "dp", y_shift(1))
    down = lax.ppermute(have, "dp", y_shift(-1))
    up2 = lax.ppermute(up, "dp", y_shift(1))
    bundle = jnp.concatenate([have, up, down, up2], axis=0)
    axes = ("dp", "expert")
    below = lax.ppermute(bundle, axes, z_shift(1))
    above = lax.ppermute(bundle, axes, z_shift(-1))
    parts = [bundle, below, above]
    parts += [lax.ppermute(p, axes, z_shift(3)) for p in (bundle, below, above)]
    parts += [lax.ppermute(p, axes, z_shift(-3)) for p in (bundle, below)]
    return jnp.concatenate(parts, axis=0)


def x_shift(step):
    return [(i, (i & 7) | ((((i >> 3) + step) % 4) << 3)) for i in range(32)]


def arranged(g, u, d, pieces):
    rows, width = g.shape
    cols = width // pieces
    stacked = jnp.stack([m.reshape(rows, pieces, cols) for m in (g, u, d)], axis=2)
    return stacked.reshape(rows, pieces * 3 * cols)


def hot_weights(w_gate, w_up, w_down, hot_id, early, late):
    groups = lax.axis_size("expert")
    replicas = lax.axis_size("dp")
    xs, zs, cores = expert_bits(groups)
    owner = hot_id[0] % groups
    share = w_gate.shape[2] // replicas
    half = share // cores
    me = lax.axis_index("expert")
    core = me % cores
    xpos = me >> 3
    base = lax.axis_index("dp") * share

    def rows_of(c):
        start = base + c * half
        g = jnp.transpose(lax.dynamic_slice_in_dim(w_gate[0], start, half, 1))
        u = jnp.transpose(lax.dynamic_slice_in_dim(w_up[0], start, half, 1))
        d = lax.dynamic_slice_in_dim(w_down[0], start, half, 0)
        return arranged(g, u, d, xs)

    own_half = rows_of(core)
    other_half = rows_of(1 - core)
    swap = [(i, i ^ 1) for i in range(groups)]
    got = lax.ppermute(other_half, "expert", swap)
    have = jnp.where((me ^ 1) == owner, got, own_half)

    rel = me ^ owner
    piece = have.shape[1] // xs
    pair = lax.dynamic_slice_in_dim(have, ((xpos >> 1) ^ 1) * 2 * piece, 2 * piece, 1)
    got = lax.ppermute(pair, "expert", [(i, i ^ 16) for i in range(groups)])
    mine_pair = lax.dynamic_slice_in_dim(have, (xpos >> 1) * 2 * piece, 2 * piece, 1)
    have = jnp.where((rel & 16) != 0, got, mine_pair)
    one = lax.dynamic_slice_in_dim(have, ((xpos ^ 1) & 1) * piece, piece, 1)
    got = lax.ppermute(one, "expert", [(i, i ^ 8) for i in range(groups)])
    mine_one = lax.dynamic_slice_in_dim(have, (xpos & 1) * piece, piece, 1)
    have = jnp.where((rel & 8) != 0, got, mine_one)

    have = early(have)

    def shifted(step):
        return [
            (i, (i & ~6) | ((((i >> 1) & 3) + step) % zs) << 1) for i in range(groups)
        ]

    distance = ((me >> 1) & 3) - ((owner >> 1) & 3)
    distance = distance % zs
    from_below = lax.ppermute(have, "expert", shifted(1))
    from_above = lax.ppermute(have, "expert", shifted(zs - 1))
    from_far = lax.ppermute(have, "expert", shifted(2))
    have = jnp.where(
        distance == 1, from_below, jnp.where(distance == zs - 1, from_above, jnp.where(distance == 2, from_far, have))
    )

    mine = gather_over_dp(have)
    left = lax.ppermute(mine, "expert", x_shift(1))
    right = lax.ppermute(mine, "expert", x_shift(-1))
    left, right = late((left, right))
    left2 = lax.ppermute(left, "expert", x_shift(1))
    held = [mine, left, right, left2]
    which = [(xpos + k) % xs for k in (0, -1, 1, -2)]
    theirs = [lax.ppermute(p, "expert", swap) for p in held]
    return held, theirs, which


def per_device(tokens, hot_gate, cold_expert, cold_gate, hot_id, w_gate, w_up, w_down):
    groups = lax.axis_size("expert")
    width = tokens.shape[1]
    dispatched = cold_expert.shape[0]
    capacity = max(2, 2 * dispatched // groups)

    cold_inputs = tokens[:dispatched]
    target = cold_expert[:, 0]
    onehot = (target[:, None] == jnp.arange(groups, dtype=jnp.int32)[None, :]).astype(jnp.int32)
    ranks_run = jnp.cumsum(onehot, axis=0)
    slot_of = jnp.sum(ranks_run * onehot, axis=1) - 1
    position = target * capacity + slot_of
    outgoing = jnp.zeros((groups * capacity, width), jnp.bfloat16).at[position].set(cold_inputs)
    outgoing = outgoing.reshape(groups, capacity, width)
    cold = {}

    def early(have):
        sent, have = lax.optimization_barrier((outgoing, have))
        received = lax.all_to_all(sent, "expert", split_axis=0, concat_axis=0, tiled=True)
        cold["served"] = expert_apply(received.reshape(-1, width), w_gate[0], w_up[0], w_down[0]).astype(jnp.bfloat16)
        return have

    def late(pieces):
        served, pieces = lax.optimization_barrier((cold["served"], pieces))
        back = lax.all_to_all(served, "expert", split_axis=0, concat_axis=0, tiled=True)
        cold["out"] = back.reshape(groups * capacity, width)[position].astype(jnp.float32)
        return pieces

    held, theirs, which = hot_weights(w_gate, w_up, w_down, hot_id, early, late)
    cold_out = cold["out"]


    cols = width // len(which)
    token_parts = [lax.dynamic_slice_in_dim(tokens, q * cols, cols, 1) for q in which]
    contract = (((1,), (1,)), ((), ()))
    outs = [None] * len(which)
    for rows in (held, theirs):
        gated = None
        upper = None
        for part, tok in zip(rows, token_parts):
            g = lax.dot_general(tok, part[:, :cols], contract, preferred_element_type=jnp.float32)
            u = lax.dot_general(tok, part[:, cols:2 * cols], contract, preferred_element_type=jnp.float32)
            gated = g if gated is None else gated + g
            upper = u if upper is None else upper + u
        hidden = (jax.nn.silu(gated) * upper).astype(jnp.bfloat16)
        for k, part in enumerate(rows):
            o = jnp.dot(hidden, part[:, 2 * cols:], preferred_element_type=jnp.float32)
            outs[k] = o if outs[k] is None else outs[k] + o
    hot_out = jnp.zeros((tokens.shape[0], width), jnp.float32)
    for q, o in zip(which, outs):
        hot_out = lax.dynamic_update_slice_in_dim(hot_out, o, q * cols, 1)

    mixed = hot_gate[:, None] * hot_out
    mixed = mixed.at[:dispatched].add(cold_gate[:, None] * cold_out)
    return mixed.astype(jnp.bfloat16)


def solution(mesh):
    return jax.shard_map(
        per_device,
        mesh=mesh,
        in_specs=(
            P(("dp", "expert"), None),
            P(("dp", "expert")),
            P(("dp", "expert"), None),
            P(("dp", "expert")),
            P(),
            P("expert", None, None),
            P("expert", None, None),
            P("expert", None, None),
        ),
        out_specs=P(("dp", "expert"), None),
        check_vma=False,
    )
```

```python
import jax
import jax.numpy as jnp
from jax import lax
from jax.sharding import PartitionSpec as P


def expert_apply(inputs, gate_mat, up_mat, down_mat):
    gated = jnp.dot(inputs, gate_mat, preferred_element_type=jnp.float32)
    upper = jnp.dot(inputs, up_mat, preferred_element_type=jnp.float32)
    hidden = (jax.nn.silu(gated) * upper).astype(jnp.bfloat16)
    return jnp.dot(hidden, down_mat, preferred_element_type=jnp.float32)


def expert_bits(count):
    return count // 8, 4, 2


def y_shift(step):
    replicas = 32
    return [(d, (d // 4) * 4 + (d % 4 + step) % 4) for d in range(replicas)]


def z_shift(step):
    pairs = []
    for d in range(32):
        for e in range(32):
            z = ((e >> 1) & 3) * 8 + d // 4
            moved = (z + step) % 32
            pairs.append((d * 32 + e, ((moved % 8) * 4 + d % 4) * 32 + ((e & ~6) | ((moved // 8) << 1))))
    return pairs


def gather_over_dp(have):
    up = lax.ppermute(have, "dp", y_shift(1))
    down = lax.ppermute(have, "dp", y_shift(-1))
    up2 = lax.ppermute(up, "dp", y_shift(1))
    bundle = jnp.concatenate([have, up, down, up2], axis=0)
    axes = ("dp", "expert")
    parts = [bundle]
    below = bundle
    above = bundle
    for step in range(4):
        below = lax.ppermute(below, axes, z_shift(1))
        parts.append(below)
        if step < 3:
            above = lax.ppermute(above, axes, z_shift(-1))
            parts.append(above)
    return jnp.concatenate(parts, axis=0)


def x_shift(step):
    return [(i, (i & 7) | ((((i >> 3) + step) % 4) << 3)) for i in range(32)]


def arranged(g, u, d, pieces):
    rows, width = g.shape
    cols = width // pieces
    stacked = jnp.stack([m.reshape(rows, pieces, cols) for m in (g, u, d)], axis=2)
    return stacked.reshape(rows, pieces * 3 * cols)


def hot_weights(w_gate, w_up, w_down, hot_id, early, middle, late):
    groups = lax.axis_size("expert")
    replicas = lax.axis_size("dp")
    xs, zs, cores = expert_bits(groups)
    owner = hot_id[0] % groups
    share = w_gate.shape[2] // replicas
    half = share // cores
    me = lax.axis_index("expert")
    core = me % cores
    xpos = me >> 3
    base = lax.axis_index("dp") * share

    g = jnp.transpose(lax.dynamic_slice_in_dim(w_gate[0], base, share, 1))
    u = jnp.transpose(lax.dynamic_slice_in_dim(w_up[0], base, share, 1))
    d = lax.dynamic_slice_in_dim(w_down[0], base, share, 0)
    whole = arranged(g, u, d, xs)
    own_half = lax.dynamic_slice_in_dim(whole, core * half, half, 0)
    other_half = lax.dynamic_slice_in_dim(whole, (1 - core) * half, half, 0)
    swap = [(i, i ^ 1) for i in range(groups)]
    got = lax.ppermute(other_half, "expert", swap)
    have = jnp.where((me ^ 1) == owner, got, own_half)

    rel = me ^ owner
    piece = have.shape[1] // xs
    pair = lax.dynamic_slice_in_dim(have, ((xpos >> 1) ^ 1) * 2 * piece, 2 * piece, 1)
    got = lax.ppermute(pair, "expert", [(i, i ^ 16) for i in range(groups)])
    mine_pair = lax.dynamic_slice_in_dim(have, (xpos >> 1) * 2 * piece, 2 * piece, 1)
    have = jnp.where((rel & 16) != 0, got, mine_pair)
    one = lax.dynamic_slice_in_dim(have, ((xpos ^ 1) & 1) * piece, piece, 1)
    got = lax.ppermute(one, "expert", [(i, i ^ 8) for i in range(groups)])
    mine_one = lax.dynamic_slice_in_dim(have, (xpos & 1) * piece, piece, 1)
    have = jnp.where((rel & 8) != 0, got, mine_one)

    have = early(have)

    def shifted(step):
        return [
            (i, (i & ~6) | ((((i >> 1) & 3) + step) % zs) << 1) for i in range(groups)
        ]

    distance = ((me >> 1) & 3) - ((owner >> 1) & 3)
    distance = distance % zs
    from_below = lax.ppermute(have, "expert", shifted(1))
    from_above = lax.ppermute(have, "expert", shifted(zs - 1))
    from_far = lax.ppermute(have, "expert", shifted(2))
    have = jnp.where(
        distance == 1, from_below, jnp.where(distance == zs - 1, from_above, jnp.where(distance == 2, from_far, have))
    )
    have = middle(have)

    mine = late(gather_over_dp(have))
    left = lax.ppermute(mine, "expert", x_shift(1))
    right = lax.ppermute(mine, "expert", x_shift(-1))
    left2 = lax.ppermute(left, "expert", x_shift(1))
    held = [mine, left, right, left2]
    which = [(xpos + k) % xs for k in (0, -1, 1, -2)]
    theirs = [lax.ppermute(p, "expert", swap) for p in held]
    return held, theirs, which


def per_device(tokens, hot_gate, cold_expert, cold_gate, hot_id, w_gate, w_up, w_down):
    groups = lax.axis_size("expert")
    width = tokens.shape[1]
    dispatched = cold_expert.shape[0]
    capacity = max(2, 2 * dispatched // groups)

    cold_inputs = tokens[:dispatched]
    target = cold_expert[:, 0]
    onehot = (target[:, None] == jnp.arange(groups, dtype=jnp.int32)[None, :]).astype(jnp.int32)
    ranks_run = jnp.cumsum(onehot, axis=0)
    slot_of = jnp.sum(ranks_run * onehot, axis=1) - 1
    position = target * capacity + slot_of
    outgoing = jnp.zeros((groups * capacity, width), jnp.bfloat16).at[position].set(cold_inputs)
    outgoing = outgoing.reshape(groups, capacity, width)
    received = lax.all_to_all(outgoing, "expert", split_axis=0, concat_axis=0, tiled=True)
    cold = {}

    def early(have):
        arrived, have = lax.optimization_barrier((received, have))
        cold["served"] = expert_apply(arrived.reshape(-1, width), w_gate[0], w_up[0], w_down[0]).astype(jnp.bfloat16)
        return have

    def middle(have):
        served, have = lax.optimization_barrier((cold["served"], have))
        cold["back"] = lax.all_to_all(
            served.reshape(received.shape), "expert", split_axis=0, concat_axis=0, tiled=True
        )
        return have

    def late(mine):
        back, mine = lax.optimization_barrier((cold["back"], mine))
        cold["out"] = back.reshape(groups * capacity, width)[position].astype(jnp.float32)
        return mine

    held, theirs, which = hot_weights(w_gate, w_up, w_down, hot_id, early, middle, late)
    cold_out = cold["out"]


    cols = width // len(which)
    token_parts = [lax.dynamic_slice_in_dim(tokens, q * cols, cols, 1) for q in which]
    contract = (((1,), (1,)), ((), ()))
    outs = [None] * len(which)
    for rows in (held, theirs):
        gated = None
        upper = None
        for part, tok in zip(rows, token_parts):
            g = lax.dot_general(tok, part[:, :cols], contract, preferred_element_type=jnp.float32)
            u = lax.dot_general(tok, part[:, cols:2 * cols], contract, preferred_element_type=jnp.float32)
            gated = g if gated is None else gated + g
            upper = u if upper is None else upper + u
        hidden = (jax.nn.silu(gated) * upper).astype(jnp.bfloat16)
        for k, part in enumerate(rows):
            o = jnp.dot(hidden, part[:, 2 * cols:], preferred_element_type=jnp.float32)
            outs[k] = o if outs[k] is None else outs[k] + o
    hot_out = jnp.zeros((tokens.shape[0], width), jnp.float32)
    for q, o in zip(which, outs):
        hot_out = lax.dynamic_update_slice_in_dim(hot_out, o, q * cols, 1)

    mixed = hot_gate[:, None] * hot_out
    mixed = mixed.at[:dispatched].add(cold_gate[:, None] * cold_out)
    return mixed.astype(jnp.bfloat16)


def solution(mesh):
    return jax.shard_map(
        per_device,
        mesh=mesh,
        in_specs=(
            P(("dp", "expert"), None),
            P(("dp", "expert")),
            P(("dp", "expert"), None),
            P(("dp", "expert")),
            P(),
            P("expert", None, None),
            P("expert", None, None),
            P("expert", None, None),
        ),
        out_specs=P(("dp", "expert"), None),
        check_vma=False,
    )
```

```python
import jax
import jax.numpy as jnp
from jax import lax
from jax.sharding import PartitionSpec as P


def expert_apply(inputs, gate_mat, up_mat, down_mat):
    gated = jnp.dot(inputs, gate_mat, preferred_element_type=jnp.float32)
    upper = jnp.dot(inputs, up_mat, preferred_element_type=jnp.float32)
    hidden = (jax.nn.silu(gated) * upper).astype(jnp.bfloat16)
    return jnp.dot(hidden, down_mat, preferred_element_type=jnp.float32)


def expert_bits(count):
    return count // 8, 4, 2


def y_shift(step):
    replicas = 32
    return [(d, (d // 4) * 4 + (d % 4 + step) % 4) for d in range(replicas)]


def z_shift(step):
    pairs = []
    for d in range(32):
        for e in range(32):
            z = ((e >> 1) & 3) * 8 + d // 4
            moved = (z + step) % 32
            pairs.append((d * 32 + e, ((moved % 8) * 4 + d % 4) * 32 + ((e & ~6) | ((moved // 8) << 1))))
    return pairs


def gather_over_dp(have):
    up = lax.ppermute(have, "dp", y_shift(1))
    down = lax.ppermute(have, "dp", y_shift(-1))
    up2 = lax.ppermute(up, "dp", y_shift(1))
    bundle = jnp.concatenate([have, up, down, up2], axis=0)
    axes = ("dp", "expert")
    parts = [bundle]
    below = bundle
    above = bundle
    for step in range(4):
        below = lax.ppermute(below, axes, z_shift(1))
        parts.append(below)
        if step < 3:
            above = lax.ppermute(above, axes, z_shift(-1))
            parts.append(above)
    return jnp.concatenate(parts, axis=0)


def x_shift(step):
    return [(i, (i & 7) | ((((i >> 3) + step) % 4) << 3)) for i in range(32)]


def arranged(g, u, d, pieces):
    rows, width = g.shape
    cols = width // pieces
    stacked = jnp.stack([m.reshape(rows, pieces, cols) for m in (g, u, d)], axis=2)
    return stacked.reshape(rows, pieces * 3 * cols)


def hot_weights(w_gate, w_up, w_down, hot_id, early, middle, late):
    groups = lax.axis_size("expert")
    replicas = lax.axis_size("dp")
    xs, zs, cores = expert_bits(groups)
    owner = hot_id[0] % groups
    share = w_gate.shape[2] // replicas
    half = share // cores
    me = lax.axis_index("expert")
    core = me % cores
    xpos = me >> 3
    base = lax.axis_index("dp") * share

    def rows_of(c):
        start = base + c * half
        g = jnp.transpose(lax.dynamic_slice_in_dim(w_gate[0], start, half, 1))
        u = jnp.transpose(lax.dynamic_slice_in_dim(w_up[0], start, half, 1))
        d = lax.dynamic_slice_in_dim(w_down[0], start, half, 0)
        return arranged(g, u, d, xs)

    own_half = rows_of(core)
    other_half = rows_of(1 - core)
    swap = [(i, i ^ 1) for i in range(groups)]
    got = lax.ppermute(other_half, "expert", swap)
    have = jnp.where((me ^ 1) == owner, got, own_half)

    rel = me ^ owner
    piece = have.shape[1] // xs
    pair = lax.dynamic_slice_in_dim(have, ((xpos >> 1) ^ 1) * 2 * piece, 2 * piece, 1)
    got = lax.ppermute(pair, "expert", [(i, i ^ 16) for i in range(groups)])
    mine_pair = lax.dynamic_slice_in_dim(have, (xpos >> 1) * 2 * piece, 2 * piece, 1)
    have = jnp.where((rel & 16) != 0, got, mine_pair)
    one = lax.dynamic_slice_in_dim(have, ((xpos ^ 1) & 1) * piece, piece, 1)
    got = lax.ppermute(one, "expert", [(i, i ^ 8) for i in range(groups)])
    mine_one = lax.dynamic_slice_in_dim(have, (xpos & 1) * piece, piece, 1)
    have = jnp.where((rel & 8) != 0, got, mine_one)


    def shifted(step):
        return [
            (i, (i & ~6) | ((((i >> 1) & 3) + step) % zs) << 1) for i in range(groups)
        ]

    distance = ((me >> 1) & 3) - ((owner >> 1) & 3)
    distance = distance % zs
    from_below = lax.ppermute(have, "expert", shifted(1))
    from_above = lax.ppermute(have, "expert", shifted(zs - 1))
    from_far = lax.ppermute(have, "expert", shifted(2))
    have = jnp.where(
        distance == 1, from_below, jnp.where(distance == zs - 1, from_above, jnp.where(distance == 2, from_far, have))
    )
    have = middle(early(have))

    mine = late(gather_over_dp(have))
    left = lax.ppermute(mine, "expert", x_shift(1))
    right = lax.ppermute(mine, "expert", x_shift(-1))
    left2 = lax.ppermute(left, "expert", x_shift(1))
    held = [mine, left, right, left2]
    which = [(xpos + k) % xs for k in (0, -1, 1, -2)]
    theirs = [lax.ppermute(p, "expert", swap) for p in held]
    return held, theirs, which


def per_device(tokens, hot_gate, cold_expert, cold_gate, hot_id, w_gate, w_up, w_down):
    groups = lax.axis_size("expert")
    width = tokens.shape[1]
    dispatched = cold_expert.shape[0]
    capacity = max(2, 2 * dispatched // groups)

    cold_inputs = tokens[:dispatched]
    target = cold_expert[:, 0]
    onehot = (target[:, None] == jnp.arange(groups, dtype=jnp.int32)[None, :]).astype(jnp.int32)
    ranks_run = jnp.cumsum(onehot, axis=0)
    slot_of = jnp.sum(ranks_run * onehot, axis=1) - 1
    position = target * capacity + slot_of
    outgoing = jnp.zeros((groups * capacity, width), jnp.bfloat16).at[position].set(cold_inputs)
    outgoing = outgoing.reshape(groups, capacity, width)
    received = lax.all_to_all(outgoing, "expert", split_axis=0, concat_axis=0, tiled=True)
    cold = {}

    def early(have):
        arrived, have = lax.optimization_barrier((received, have))
        cold["served"] = expert_apply(arrived.reshape(-1, width), w_gate[0], w_up[0], w_down[0]).astype(jnp.bfloat16)
        return have

    def middle(have):
        served, have = lax.optimization_barrier((cold["served"], have))
        cold["back"] = lax.all_to_all(
            served.reshape(received.shape), "expert", split_axis=0, concat_axis=0, tiled=True
        )
        return have

    def late(mine):
        back, mine = lax.optimization_barrier((cold["back"], mine))
        cold["out"] = back.reshape(groups * capacity, width)[position].astype(jnp.float32)
        return mine

    held, theirs, which = hot_weights(w_gate, w_up, w_down, hot_id, early, middle, late)
    cold_out = cold["out"]


    cols = width // len(which)
    token_parts = [lax.dynamic_slice_in_dim(tokens, q * cols, cols, 1) for q in which]
    contract = (((1,), (1,)), ((), ()))
    outs = [None] * len(which)
    for rows in (held, theirs):
        gated = None
        upper = None
        for part, tok in zip(rows, token_parts):
            g = lax.dot_general(tok, part[:, :cols], contract, preferred_element_type=jnp.float32)
            u = lax.dot_general(tok, part[:, cols:2 * cols], contract, preferred_element_type=jnp.float32)
            gated = g if gated is None else gated + g
            upper = u if upper is None else upper + u
        hidden = (jax.nn.silu(gated) * upper).astype(jnp.bfloat16)
        for k, part in enumerate(rows):
            o = jnp.dot(hidden, part[:, 2 * cols:], preferred_element_type=jnp.float32)
            outs[k] = o if outs[k] is None else outs[k] + o
    hot_out = jnp.zeros((tokens.shape[0], width), jnp.float32)
    for q, o in zip(which, outs):
        hot_out = lax.dynamic_update_slice_in_dim(hot_out, o, q * cols, 1)

    mixed = hot_gate[:, None] * hot_out
    mixed = mixed.at[:dispatched].add(cold_gate[:, None] * cold_out)
    return mixed.astype(jnp.bfloat16)


def solution(mesh):
    return jax.shard_map(
        per_device,
        mesh=mesh,
        in_specs=(
            P(("dp", "expert"), None),
            P(("dp", "expert")),
            P(("dp", "expert"), None),
            P(("dp", "expert")),
            P(),
            P("expert", None, None),
            P("expert", None, None),
            P("expert", None, None),
        ),
        out_specs=P(("dp", "expert"), None),
        check_vma=False,
    )
```

```python
import jax
import jax.numpy as jnp
from jax import lax
from jax.sharding import PartitionSpec as P


def expert_apply(inputs, gate_mat, up_mat, down_mat):
    gated = jnp.dot(inputs, gate_mat, preferred_element_type=jnp.float32)
    upper = jnp.dot(inputs, up_mat, preferred_element_type=jnp.float32)
    hidden = (jax.nn.silu(gated) * upper).astype(jnp.bfloat16)
    return jnp.dot(hidden, down_mat, preferred_element_type=jnp.float32)


def expert_bits(count):
    return count // 8, 4, 2


def y_shift(step):
    replicas = 32
    return [(d, (d // 4) * 4 + (d % 4 + step) % 4) for d in range(replicas)]


def z_shift(step):
    pairs = []
    for d in range(32):
        for e in range(32):
            z = ((e >> 1) & 3) * 8 + d // 4
            moved = (z + step) % 32
            pairs.append((d * 32 + e, ((moved % 8) * 4 + d % 4) * 32 + ((e & ~6) | ((moved // 8) << 1))))
    return pairs


def gather_over_dp(have):
    near = lax.ppermute(have, "dp", y_shift(1))
    pair = jnp.concatenate([have, near], axis=0)
    far = lax.ppermute(pair, "dp", y_shift(2))
    bundle = jnp.concatenate([pair, far], axis=0)
    axes = ("dp", "expert")
    below = lax.ppermute(bundle, axes, z_shift(1))
    two = jnp.concatenate([bundle, below], axis=0)
    below2 = lax.ppermute(two, axes, z_shift(2))
    from_below = lax.ppermute(two, axes, z_shift(4))
    from_above = lax.ppermute(below2, axes, z_shift(-4))
    return jnp.concatenate([two, below2, from_below, from_above], axis=0)


def x_shift(step):
    return [(i, (i & 7) | ((((i >> 3) + step) % 4) << 3)) for i in range(32)]


def arranged(g, u, d, pieces):
    rows, width = g.shape
    cols = width // pieces
    stacked = jnp.stack([m.reshape(rows, pieces, cols) for m in (g, u, d)], axis=2)
    return stacked.reshape(rows, pieces * 3 * cols)


def hot_weights(w_gate, w_up, w_down, hot_id, early, middle, late):
    groups = lax.axis_size("expert")
    replicas = lax.axis_size("dp")
    xs, zs, cores = expert_bits(groups)
    owner = hot_id[0] % groups
    share = w_gate.shape[2] // replicas
    half = share // cores
    me = lax.axis_index("expert")
    core = me % cores
    xpos = me >> 3
    base = lax.axis_index("dp") * share

    def rows_of(c):
        start = base + c * half
        g = jnp.transpose(lax.dynamic_slice_in_dim(w_gate[0], start, half, 1))
        u = jnp.transpose(lax.dynamic_slice_in_dim(w_up[0], start, half, 1))
        d = lax.dynamic_slice_in_dim(w_down[0], start, half, 0)
        return arranged(g, u, d, xs)

    own_half = rows_of(core)
    other_half = rows_of(1 - core)
    swap = [(i, i ^ 1) for i in range(groups)]
    got = lax.ppermute(other_half, "expert", swap)
    have = jnp.where((me ^ 1) == owner, got, own_half)

    rel = me ^ owner
    piece = have.shape[1] // xs
    pair = lax.dynamic_slice_in_dim(have, ((xpos >> 1) ^ 1) * 2 * piece, 2 * piece, 1)
    got = lax.ppermute(pair, "expert", [(i, i ^ 16) for i in range(groups)])
    mine_pair = lax.dynamic_slice_in_dim(have, (xpos >> 1) * 2 * piece, 2 * piece, 1)
    have = jnp.where((rel & 16) != 0, got, mine_pair)
    one = lax.dynamic_slice_in_dim(have, ((xpos ^ 1) & 1) * piece, piece, 1)
    got = lax.ppermute(one, "expert", [(i, i ^ 8) for i in range(groups)])
    mine_one = lax.dynamic_slice_in_dim(have, (xpos & 1) * piece, piece, 1)
    have = jnp.where((rel & 8) != 0, got, mine_one)


    def shifted(step):
        return [
            (i, (i & ~6) | ((((i >> 1) & 3) + step) % zs) << 1) for i in range(groups)
        ]

    distance = ((me >> 1) & 3) - ((owner >> 1) & 3)
    distance = distance % zs
    from_below = lax.ppermute(have, "expert", shifted(1))
    from_above = lax.ppermute(have, "expert", shifted(zs - 1))
    from_far = lax.ppermute(have, "expert", shifted(2))
    have = jnp.where(
        distance == 1, from_below, jnp.where(distance == zs - 1, from_above, jnp.where(distance == 2, from_far, have))
    )
    have = middle(early(have))

    mine = late(gather_over_dp(have))
    left = lax.ppermute(mine, "expert", x_shift(1))
    right = lax.ppermute(mine, "expert", x_shift(-1))
    left2 = lax.ppermute(left, "expert", x_shift(1))
    held = [mine, left, right, left2]
    which = [(xpos + k) % xs for k in (0, -1, 1, -2)]
    theirs = [lax.ppermute(p, "expert", swap) for p in held]
    return held, theirs, which


def per_device(tokens, hot_gate, cold_expert, cold_gate, hot_id, w_gate, w_up, w_down):
    groups = lax.axis_size("expert")
    width = tokens.shape[1]
    dispatched = cold_expert.shape[0]
    capacity = max(2, 2 * dispatched // groups)

    cold_inputs = tokens[:dispatched]
    target = cold_expert[:, 0]
    onehot = (target[:, None] == jnp.arange(groups, dtype=jnp.int32)[None, :]).astype(jnp.int32)
    ranks_run = jnp.cumsum(onehot, axis=0)
    slot_of = jnp.sum(ranks_run * onehot, axis=1) - 1
    position = target * capacity + slot_of
    outgoing = jnp.zeros((groups * capacity, width), jnp.bfloat16).at[position].set(cold_inputs)
    outgoing = outgoing.reshape(groups, capacity, width)
    received = lax.all_to_all(outgoing, "expert", split_axis=0, concat_axis=0, tiled=True)
    cold = {}

    def early(have):
        arrived, have = lax.optimization_barrier((received, have))
        cold["served"] = expert_apply(arrived.reshape(-1, width), w_gate[0], w_up[0], w_down[0]).astype(jnp.bfloat16)
        return have

    def middle(have):
        served, have = lax.optimization_barrier((cold["served"], have))
        cold["back"] = lax.all_to_all(
            served.reshape(received.shape), "expert", split_axis=0, concat_axis=0, tiled=True
        )
        return have

    def late(mine):
        back, mine = lax.optimization_barrier((cold["back"], mine))
        cold["out"] = back.reshape(groups * capacity, width)[position].astype(jnp.float32)
        return mine

    held, theirs, which = hot_weights(w_gate, w_up, w_down, hot_id, early, middle, late)
    cold_out = cold["out"]


    cols = width // len(which)
    token_parts = [lax.dynamic_slice_in_dim(tokens, q * cols, cols, 1) for q in which]
    contract = (((1,), (1,)), ((), ()))
    outs = [None] * len(which)
    for rows in (held, theirs):
        gated = None
        upper = None
        for part, tok in zip(rows, token_parts):
            g = lax.dot_general(tok, part[:, :cols], contract, preferred_element_type=jnp.float32)
            u = lax.dot_general(tok, part[:, cols:2 * cols], contract, preferred_element_type=jnp.float32)
            gated = g if gated is None else gated + g
            upper = u if upper is None else upper + u
        hidden = (jax.nn.silu(gated) * upper).astype(jnp.bfloat16)
        for k, part in enumerate(rows):
            o = jnp.dot(hidden, part[:, 2 * cols:], preferred_element_type=jnp.float32)
            outs[k] = o if outs[k] is None else outs[k] + o
    hot_out = jnp.zeros((tokens.shape[0], width), jnp.float32)
    for q, o in zip(which, outs):
        hot_out = lax.dynamic_update_slice_in_dim(hot_out, o, q * cols, 1)

    mixed = hot_gate[:, None] * hot_out
    mixed = mixed.at[:dispatched].add(cold_gate[:, None] * cold_out)
    return mixed.astype(jnp.bfloat16)


def solution(mesh):
    return jax.shard_map(
        per_device,
        mesh=mesh,
        in_specs=(
            P(("dp", "expert"), None),
            P(("dp", "expert")),
            P(("dp", "expert"), None),
            P(("dp", "expert")),
            P(),
            P("expert", None, None),
            P("expert", None, None),
            P("expert", None, None),
        ),
        out_specs=P(("dp", "expert"), None),
        check_vma=False,
    )
```

```python
import jax
import jax.numpy as jnp
from jax import lax
from jax.sharding import PartitionSpec as P


def expert_apply(inputs, gate_mat, up_mat, down_mat):
    gated = jnp.dot(inputs, gate_mat, preferred_element_type=jnp.float32)
    upper = jnp.dot(inputs, up_mat, preferred_element_type=jnp.float32)
    hidden = (jax.nn.silu(gated) * upper).astype(jnp.bfloat16)
    return jnp.dot(hidden, down_mat, preferred_element_type=jnp.float32)


def expert_bits(count):
    return count // 8, 4, 2


def y_shift(step):
    replicas = 32
    return [(d, (d // 4) * 4 + (d % 4 + step) % 4) for d in range(replicas)]


def z_shift(step):
    pairs = []
    for d in range(32):
        for e in range(32):
            z = ((e >> 1) & 3) * 8 + d // 4
            moved = (z + step) % 32
            pairs.append((d * 32 + e, ((moved % 8) * 4 + d % 4) * 32 + ((e & ~6) | ((moved // 8) << 1))))
    return pairs


def gather_over_dp(have):
    up = lax.ppermute(have, "dp", y_shift(1))
    down = lax.ppermute(have, "dp", y_shift(-1))
    up2 = lax.ppermute(up, "dp", y_shift(1))
    bundle = jnp.concatenate([have, up, down, up2], axis=0)
    axes = ("dp", "expert")
    parts = [bundle]
    below = bundle
    above = bundle
    for step in range(4):
        below = lax.ppermute(below, axes, z_shift(1))
        parts.append(below)
        if step < 3:
            above = lax.ppermute(above, axes, z_shift(-1))
            parts.append(above)
    return jnp.concatenate(parts, axis=0)


def x_shift(step):
    return [(i, (i & 7) | ((((i >> 3) + step) % 4) << 3)) for i in range(32)]


def arranged(g, u, d, pieces):
    rows, width = g.shape
    cols = width // pieces
    stacked = jnp.stack([m.reshape(rows, pieces, cols) for m in (g, u, d)], axis=2)
    return stacked.reshape(rows, pieces * 3 * cols)


def hot_weights(w_gate, w_up, w_down, hot_id, early, middle, late):
    groups = lax.axis_size("expert")
    replicas = lax.axis_size("dp")
    xs, zs, cores = expert_bits(groups)
    owner = hot_id[0] % groups
    share = w_gate.shape[2] // replicas
    half = share // cores
    me = lax.axis_index("expert")
    core = me % cores
    xpos = me >> 3
    base = lax.axis_index("dp") * share

    g = jnp.transpose(lax.dynamic_slice_in_dim(w_gate[0], base, share, 1))
    u = jnp.transpose(lax.dynamic_slice_in_dim(w_up[0], base, share, 1))
    d = lax.dynamic_slice_in_dim(w_down[0], base, share, 0)
    whole = arranged(g, u, d, xs)
    own_half = lax.dynamic_slice_in_dim(whole, core * half, half, 0)
    other_half = lax.dynamic_slice_in_dim(whole, (1 - core) * half, half, 0)
    swap = [(i, i ^ 1) for i in range(groups)]
    got = lax.ppermute(other_half, "expert", swap)
    have = jnp.where((me ^ 1) == owner, got, own_half)

    rel = me ^ owner
    piece = have.shape[1] // xs
    pair = lax.dynamic_slice_in_dim(have, ((xpos >> 1) ^ 1) * 2 * piece, 2 * piece, 1)
    got = lax.ppermute(pair, "expert", [(i, i ^ 16) for i in range(groups)])
    mine_pair = lax.dynamic_slice_in_dim(have, (xpos >> 1) * 2 * piece, 2 * piece, 1)
    have = jnp.where((rel & 16) != 0, got, mine_pair)
    one = lax.dynamic_slice_in_dim(have, ((xpos ^ 1) & 1) * piece, piece, 1)
    got = lax.ppermute(one, "expert", [(i, i ^ 8) for i in range(groups)])
    mine_one = lax.dynamic_slice_in_dim(have, (xpos & 1) * piece, piece, 1)
    have = jnp.where((rel & 8) != 0, got, mine_one)


    def shifted(step):
        return [
            (i, (i & ~6) | ((((i >> 1) & 3) + step) % zs) << 1) for i in range(groups)
        ]

    distance = ((me >> 1) & 3) - ((owner >> 1) & 3)
    distance = distance % zs
    from_below = lax.ppermute(have, "expert", shifted(1))
    from_above = lax.ppermute(have, "expert", shifted(zs - 1))
    from_far = lax.ppermute(have, "expert", shifted(2))
    have = jnp.where(
        distance == 1, from_below, jnp.where(distance == zs - 1, from_above, jnp.where(distance == 2, from_far, have))
    )
    have = middle(early(have))

    mine = late(gather_over_dp(have))
    left = lax.ppermute(mine, "expert", x_shift(1))
    right = lax.ppermute(mine, "expert", x_shift(-1))
    left2 = lax.ppermute(left, "expert", x_shift(1))
    held = [mine, left, right, left2]
    which = [(xpos + k) % xs for k in (0, -1, 1, -2)]
    theirs = [lax.ppermute(p, "expert", swap) for p in held]
    return held, theirs, which


def per_device(tokens, hot_gate, cold_expert, cold_gate, hot_id, w_gate, w_up, w_down):
    groups = lax.axis_size("expert")
    width = tokens.shape[1]
    dispatched = cold_expert.shape[0]
    capacity = max(2, 2 * dispatched // groups)

    cold_inputs = tokens[:dispatched]
    target = cold_expert[:, 0]
    onehot = (target[:, None] == jnp.arange(groups, dtype=jnp.int32)[None, :]).astype(jnp.int32)
    ranks_run = jnp.cumsum(onehot, axis=0)
    slot_of = jnp.sum(ranks_run * onehot, axis=1) - 1
    position = target * capacity + slot_of
    outgoing = jnp.zeros((groups * capacity, width), jnp.bfloat16).at[position].set(cold_inputs)
    outgoing = outgoing.reshape(groups, capacity, width)
    received = lax.all_to_all(outgoing, "expert", split_axis=0, concat_axis=0, tiled=True)
    cold = {}

    def early(have):
        arrived, have = lax.optimization_barrier((received, have))
        cold["served"] = expert_apply(arrived.reshape(-1, width), w_gate[0], w_up[0], w_down[0]).astype(jnp.bfloat16)
        return have

    def middle(have):
        served, have = lax.optimization_barrier((cold["served"], have))
        cold["back"] = lax.all_to_all(
            served.reshape(received.shape), "expert", split_axis=0, concat_axis=0, tiled=True
        )
        return have

    def late(mine):
        back, mine = lax.optimization_barrier((cold["back"], mine))
        cold["out"] = back.reshape(groups * capacity, width)[position].astype(jnp.float32)
        return mine

    held, theirs, which = hot_weights(w_gate, w_up, w_down, hot_id, early, middle, late)
    cold_out = cold["out"]


    cols = width // len(which)
    token_parts = [lax.dynamic_slice_in_dim(tokens, q * cols, cols, 1) for q in which]
    contract = (((1,), (1,)), ((), ()))
    outs = [None] * len(which)
    for rows in (held, theirs):
        gated = None
        upper = None
        for part, tok in zip(rows, token_parts):
            g = lax.dot_general(tok, part[:, :cols], contract, preferred_element_type=jnp.float32)
            u = lax.dot_general(tok, part[:, cols:2 * cols], contract, preferred_element_type=jnp.float32)
            gated = g if gated is None else gated + g
            upper = u if upper is None else upper + u
        hidden = (jax.nn.silu(gated) * upper).astype(jnp.bfloat16)
        for k, part in enumerate(rows):
            o = jnp.dot(hidden, part[:, 2 * cols:], preferred_element_type=jnp.float32)
            outs[k] = o if outs[k] is None else outs[k] + o
    hot_out = jnp.zeros((tokens.shape[0], width), jnp.float32)
    for q, o in zip(which, outs):
        hot_out = lax.dynamic_update_slice_in_dim(hot_out, o, q * cols, 1)

    mixed = hot_gate[:, None] * hot_out
    mixed = mixed.at[:dispatched].add(cold_gate[:, None] * cold_out)
    return mixed.astype(jnp.bfloat16)


def solution(mesh):
    return jax.shard_map(
        per_device,
        mesh=mesh,
        in_specs=(
            P(("dp", "expert"), None),
            P(("dp", "expert")),
            P(("dp", "expert"), None),
            P(("dp", "expert")),
            P(),
            P("expert", None, None),
            P("expert", None, None),
            P("expert", None, None),
        ),
        out_specs=P(("dp", "expert"), None),
        check_vma=False,
    )
```
